256 devices in a mesh: req: 32 (over x, y, core), kv: 8 (over z).
Axes of the slice: x: 4, y: 4, z: 8, core: 2. Of those that a mesh axis runs over, the one named last changes fastest.
Arguments:
- hidden: bfloat16 [512, 1536], P('req'), may hold values from -6 to 6
- norm_gain: float32 [1536], replicated, may hold values from 0.5 to 1.5
- w_qkv: bfloat16 [1536, 3072], P(None, 'kv'), may hold values from -0.15625 to 0.15625
- w_out: bfloat16 [1536, 1536], P(None, 'kv'), may hold values from -0.15625 to 0.15625
- cache_pages: bfloat16 [6144, 2, 8, 96, 128], P('req', None, 'kv'), may hold values from -340 to 340
- lengths: int32 [512], P('req'), may hold values from 1 to 16384, as said below
- page_table: int32 [512, 128], P('req'), may hold values from 0 to 191, as said below
- occupant: int32 [512], replicated, may hold values from 0 to 511, each once
Outputs:
- mixed: bfloat16 [512, 1536], P('req', 'kv')
The draws below stay inside these ranges and needn't reach their ends.
Inputs may be any that keep to these rules, and one draw needn't show every extreme that they name: `occupant`: every request is served at exactly one slot. Slot s holds ceil(lengths[s] / 128) pages; on every index of req the pages of its 16 slots fit its pool of 192, some pool is full, and some request has 16384 tokens. `page_table`: the first ceil(lengths[s] / 128) entries of slot s are pages of its own pool that no other slot of that pool uses; later entries are arbitrary pages of the pool.
All inputs are finite; a program needn't handle non-finite values.
Results may differ from the reference program's by a relative error of at most 0.0043.
Values may be sent and summed in bfloat16 or wider, within the bound.
No kernel may reach another device: no remote copies, remote signals or barrier semaphores. Data moves between devices by JAX's collectives and lax.ppermute only.
A program may use at most 64 MiB of HBM per device.

```python
import math
import jax
import jax.numpy as jnp
from jax import lax

D = 1536
HQ = 16
KVH = 8
HD = 96
PAGE = 128
MAXP = 128
REQ_DEV = 16
GROUP = 2
QKV = 3072
REQUESTS = 512
PAGES_DEV = 192
NPAGES = 6144


def page_plan(key):
    device_count = REQUESTS // REQ_DEV
    pool_size = MAXP + 4 * REQ_DEV
    key_full, key_slot, key_budget, key_weight, key_tail, key_perm, key_junk = jax.random.split(jax.random.fold_in(key, 7), 7)
    full_device = jax.random.randint(key_full, (), 0, device_count)
    big_slot = jax.random.randint(key_slot, (), 0, REQ_DEV)
    helper_slot = (big_slot + 1) % REQ_DEV
    device_ids = jnp.arange(device_count, dtype=jnp.int32)[:, None]
    slot_ids = jnp.arange(REQ_DEV, dtype=jnp.int32)[None, :]
    budget = jax.random.randint(key_budget, (device_count, 1), REQ_DEV, pool_size // 2 + 1)
    exponent = jax.random.randint(key_weight, (device_count, REQ_DEV), 0, 8)
    weight = jnp.left_shift(jnp.ones_like(exponent), exponent)
    extra_pages = weight * (budget - REQ_DEV) // jnp.sum(weight, axis=1, keepdims=True)
    page_count = jnp.minimum(1 + extra_pages, MAXP)
    full_count = jnp.where(slot_ids == big_slot, MAXP, jnp.where(slot_ids == helper_slot, 8, 4))
    page_count = jnp.where(device_ids == full_device, full_count, page_count)
    tail_fill = jax.random.randint(key_tail, (device_count, REQ_DEV), 1, PAGE + 1)
    big_mask = (device_ids == full_device) & (slot_ids == big_slot)
    tail_fill = jnp.where(big_mask, PAGE, tail_fill)
    lengths = (page_count - 1) * PAGE + tail_fill
    starts = jnp.cumsum(page_count, axis=1) - page_count

    def shuffle(sub_key):
        return jax.random.permutation(sub_key, pool_size)
    orders = jax.vmap(shuffle)(jax.random.split(key_perm, device_count))
    ranks = jnp.arange(MAXP, dtype=jnp.int32)[None, None, :]
    position = jnp.minimum(starts[:, :, None] + ranks, pool_size - 1)
    chosen = jnp.take(orders.reshape(-1), device_ids[:, :, None] * pool_size + position)
    junk = jax.random.randint(key_junk, (device_count, REQ_DEV, MAXP), 0, pool_size)
    table = jnp.where(ranks < page_count[:, :, None], chosen, junk)
    return (lengths.reshape(-1).astype(jnp.int32), table.reshape(REQUESTS, MAXP).astype(jnp.int32))


def draw_lengths(key, part):
    return page_plan(key)[0]


def draw_page_table(key, part):
    return page_plan(key)[1]


def draw_cache_pages(key, part):
    key_body = jax.random.fold_in(jax.random.fold_in(key, 11), 0)
    shape = (NPAGES, 2, KVH, HD, PAGE)
    kind_index = jnp.arange(2).reshape(1, 2, 1, 1, 1)
    raw = jnp.clip(jax.random.normal(key_body, shape, jnp.float32), -4.0, 4.0)
    boost = jnp.ones((NPAGES, 1, 1, 1, 1), jnp.float32)
    factor = jnp.where(kind_index == 0, 2.5 * boost, 1.0)
    return (raw * factor).astype(jnp.bfloat16)


def block_scale(rng, extent, cuts, low, largest):
    def one(dim, blocks):
        draws = jax.random.uniform(jax.random.fold_in(jax.random.fold_in(rng, 6), dim), (blocks,), jnp.float32, low / len(cuts), largest / len(cuts))
        return jnp.repeat(jnp.exp(draws), extent[dim] // blocks).reshape((-1,) + (1,) * (len(extent) - dim - 1))

    loudness = one(*cuts[0])
    for cut in cuts[1:]:
        loudness = loudness * one(*cut)
    return loudness


def normal_values(rng, shape, scale, bound, pieces=(), kind=jnp.bfloat16):
    values = scale * jax.random.normal(rng, shape, jnp.float32)
    if pieces:
        values = values * block_scale(rng, shape, pieces, -0.22, 0.18)
    return jnp.clip(values, -bound, bound).astype(kind)


def setup_inputs(seed: int = 0) -> dict:
    key_of = jax.random.split(jax.random.key(seed), 9)
    return {
        "hidden": normal_values(key_of[0], (REQUESTS, D), 1.0, 6.0, ((0, 32),)),
        "norm_gain": jnp.clip(1.0 + 0.1 * jax.random.normal(key_of[1], (D,), jnp.float32), 0.5, 1.5),
        "w_qkv": normal_values(key_of[2], (D, QKV), D ** -0.5, 0.15625, ((1, 8),)),
        "w_out": normal_values(key_of[3], (D, HQ * HD), (HQ * HD) ** -0.5, 0.15625, ((1, 8),)),
        "cache_pages": draw_cache_pages(jax.random.fold_in(key_of[8], 71), 0),
        "lengths": draw_lengths(jax.random.fold_in(key_of[8], 71), 0),
        "page_table": draw_page_table(jax.random.fold_in(key_of[8], 71), 0),
        "occupant": jax.random.permutation(key_of[7], REQUESTS).astype(jnp.int32),
    }


def reference(hidden, norm_gain, w_qkv, w_out, cache_pages, lengths, page_table, occupant):
    hidden_wide = hidden.astype(jnp.float32)
    normed = (hidden_wide * lax.rsqrt(lax.optimization_barrier(jnp.mean(hidden_wide * hidden_wide, axis=1, keepdims=True)) + 1e-05) * norm_gain).astype(jnp.bfloat16)
    projections = jnp.dot(normed, w_qkv, preferred_element_type=jnp.float32).astype(jnp.bfloat16)
    slot_rows = jnp.take(projections, occupant, axis=0).reshape(REQUESTS, KVH, GROUP + 2, HD)
    score_scale = 1.0 / math.sqrt(HD)
    positions = jnp.arange(MAXP * PAGE, dtype=jnp.int32)

    def one_slot(slot_index):
        slot_entry = slot_rows[slot_index].astype(jnp.float32)
        queries = slot_entry[:, :GROUP]
        own_key = slot_entry[:, GROUP]
        own_value = slot_entry[:, GROUP + 1]
        pool_base = slot_index // REQ_DEV * PAGES_DEV
        gathered_pages = jnp.take(cache_pages, page_table[slot_index] + pool_base, axis=0).astype(jnp.float32)
        key_rows = jnp.transpose(gathered_pages[:, 0], (1, 2, 0, 3)).reshape(KVH, HD, MAXP * PAGE)
        values = jnp.transpose(gathered_pages[:, 1], (1, 2, 0, 3)).reshape(KVH, HD, MAXP * PAGE)
        scores = jnp.einsum('gjd,gdt->gjt', queries, key_rows) * score_scale
        token_live = positions < lengths[slot_index]
        scores = jnp.where(token_live[None, None, :], scores, -jnp.inf)
        own_score = lax.optimization_barrier(jnp.sum(queries * own_key[:, None, :], axis=-1)) * score_scale
        slot_max = jnp.maximum(lax.optimization_barrier(jnp.max(scores, axis=-1)), own_score)
        weights = jnp.exp(scores - slot_max[..., None])
        own_weight = jnp.exp(own_score - slot_max)
        denominator = lax.optimization_barrier(jnp.sum(weights, axis=-1)) + own_weight
        rounded = lax.optimization_barrier(weights.astype(jnp.bfloat16)).astype(jnp.float32)
        own_rounded = lax.optimization_barrier(own_weight.astype(jnp.bfloat16)).astype(jnp.float32)
        numerator = jnp.einsum('gjt,gdt->gjd', rounded, values) + own_rounded[..., None] * own_value[:, None, :]
        return (numerator / denominator[..., None]).astype(jnp.bfloat16).reshape(HQ * HD)
    context = lax.map(one_slot, jnp.arange(REQUESTS, dtype=jnp.int32))
    inverse = jnp.zeros((REQUESTS,), jnp.int32).at[occupant].set(jnp.arange(REQUESTS, dtype=jnp.int32))
    attended = jnp.take(context, inverse, axis=0)
    projected = jnp.dot(attended, w_out.T, preferred_element_type=jnp.float32)
    return (hidden_wide + projected).astype(jnp.bfloat16)
```

```python
import math

import jax
import jax.numpy as jnp
from jax import lax
from jax.sharding import PartitionSpec as P

HD = 96
PAGE = 128
MAXP = 128
GROUP = 2


def per_device(hidden, norm_gain, w_qkv, w_out, cache_pages, lengths, page_table, occupant):
    slot_count = hidden.shape[0]
    pool_size = cache_pages.shape[0]
    kv_local = cache_pages.shape[2]
    first_slot = lax.axis_index("req") * slot_count
    hidden_wide = hidden.astype(jnp.float32)
    normed = (
        hidden_wide
        * lax.rsqrt(jnp.mean(hidden_wide * hidden_wide, axis=1, keepdims=True) + 1e-05)
        * norm_gain
    ).astype(jnp.bfloat16)
    served = lax.dynamic_slice_in_dim(occupant, first_slot, slot_count)
    own_rows = jnp.dot(normed, w_qkv, preferred_element_type=jnp.float32).astype(jnp.bfloat16)
    every_row = lax.all_gather(own_rows, "req", axis=0, tiled=True)
    slot_rows = jnp.take(every_row, served, axis=0)
    slot_rows = slot_rows.reshape(slot_count, kv_local, GROUP + 2, HD)
    queries = slot_rows[:, :, :GROUP]
    own_key = slot_rows[:, :, GROUP]
    own_value = slot_rows[:, :, GROUP + 1]
    score_scale = 1.0 / math.sqrt(HD)
    pages_used = (lengths + PAGE - 1) // PAGE
    live_page = jnp.arange(MAXP, dtype=jnp.int32)[None, :] < pages_used[:, None]
    matches = (
        (page_table[:, :, None] == jnp.arange(pool_size, dtype=jnp.int32)[None, None, :])
        & live_page[:, :, None]
    ).astype(jnp.int32)
    owner_table = jnp.sum(matches, axis=1)
    slot_ids = jnp.arange(slot_count, dtype=jnp.int32)
    page_owner = jnp.sum(owner_table * slot_ids[:, None], axis=0)
    page_rank = jnp.sum(matches * jnp.arange(MAXP, dtype=jnp.int32)[None, :, None], axis=(0, 1))
    page_limit = jnp.sum(owner_table * lengths[:, None], axis=0)
    offsets = page_rank[:, None] * PAGE + jnp.arange(PAGE, dtype=jnp.int32)[None, :]
    token_live = offsets < page_limit[:, None]
    page_queries = jnp.take(queries, page_owner, axis=0)
    scores = (
        jnp.einsum(
            "pgjd,pgdt->pgjt", page_queries, cache_pages[:, 0], preferred_element_type=jnp.float32
        )
        * score_scale
    )
    scores = jnp.where(token_live[:, None, None, :], scores, -jnp.inf)
    page_max = jnp.max(scores, axis=-1)
    own_score = (
        jnp.sum(queries.astype(jnp.float32) * own_key.astype(jnp.float32)[:, :, None, :], axis=-1)
        * score_scale
    )
    owner_mask = owner_table > 0
    slot_max = jnp.max(jnp.where(owner_mask[:, :, None, None], page_max[None], -jnp.inf), axis=1)
    slot_max = jnp.maximum(slot_max, own_score)
    weights = jnp.exp(scores - jnp.take(slot_max, page_owner, axis=0)[..., None])
    rounded = weights.astype(jnp.bfloat16)
    page_total = jnp.sum(weights, axis=-1)
    page_numerator = jnp.einsum(
        "pgjt,pgdt->pgjd", rounded, cache_pages[:, 1], preferred_element_type=jnp.float32
    )
    own_weight = jnp.exp(own_score - slot_max)
    own_rounded = lax.optimization_barrier(own_weight.astype(jnp.bfloat16)).astype(jnp.float32)
    owner_float = owner_table.astype(jnp.float32)
    denominator = (
        jnp.einsum("sp,pgj->sgj", owner_float, page_total, precision=lax.Precision.HIGHEST)
        + own_weight
    )
    numerator = jnp.einsum(
        "sp,pgjd->sgjd", owner_float, page_numerator, precision=lax.Precision.HIGHEST
    )
    numerator = numerator + own_rounded[..., None] * own_value.astype(jnp.float32)[:, :, None, :]
    context = (numerator / denominator[..., None]).astype(jnp.bfloat16).reshape(slot_count, -1)
    gathered = lax.all_gather(context, "req", axis=0, tiled=True)
    wanted = first_slot + slot_ids
    selector = (occupant[None, :] == wanted[:, None]).astype(jnp.bfloat16)
    attended = jnp.dot(selector, gathered, preferred_element_type=jnp.float32).astype(jnp.bfloat16)
    partial_value = lax.dot_general(
        attended, w_out, (((1,), (1,)), ((), ())), preferred_element_type=jnp.float32
    )
    summed = lax.psum_scatter(partial_value, "kv", scatter_dimension=1, tiled=True)
    col_share = summed.shape[1]
    residual = lax.dynamic_slice_in_dim(hidden_wide, lax.axis_index("kv") * col_share, col_share, 1)
    return (residual + summed).astype(jnp.bfloat16)


def solution(mesh):
    return jax.shard_map(
        per_device,
        mesh=mesh,
        in_specs=(
            P("req", None),
            P(),
            P(None, "kv"),
            P(None, "kv"),
            P("req", None, "kv", None, None),
            P("req"),
            P("req", None),
            P(),
        ),
        out_specs=P("req", "kv"),
        check_vma=False,
    )
```

```python
import math

import jax
import jax.numpy as jnp
from jax import lax
from jax.sharding import PartitionSpec as P

HD = 96
PAGE = 128
MAXP = 128
GROUP = 2


def exchange(rows, axis):
    count = lax.axis_size(axis)
    sent = jnp.broadcast_to(rows[None], (count,) + rows.shape)
    return lax.all_to_all(sent, axis, 0, 0).reshape(count * rows.shape[0], rows.shape[1])


def per_device(hidden, norm_gain, w_qkv, w_out, cache_pages, lengths, page_table, occupant):
    slot_count = hidden.shape[0]
    pool_size = cache_pages.shape[0]
    kv_local = cache_pages.shape[2]
    first_slot = lax.axis_index("req") * slot_count
    hidden_wide = hidden.astype(jnp.float32)
    normed = (
        hidden_wide
        * lax.rsqrt(jnp.mean(hidden_wide * hidden_wide, axis=1, keepdims=True) + 1e-05)
        * norm_gain
    ).astype(jnp.bfloat16)
    served = lax.dynamic_slice_in_dim(occupant, first_slot, slot_count)
    own_rows = jnp.dot(normed, w_qkv, preferred_element_type=jnp.float32).astype(jnp.bfloat16)
    every_row = exchange(own_rows, "req")
    slot_rows = jnp.take(every_row, served, axis=0)
    slot_rows = slot_rows.reshape(slot_count, kv_local, GROUP + 2, HD)
    queries = slot_rows[:, :, :GROUP]
    own_key = slot_rows[:, :, GROUP]
    own_value = slot_rows[:, :, GROUP + 1]
    score_scale = 1.0 / math.sqrt(HD)
    pages_used = (lengths + PAGE - 1) // PAGE
    live_page = jnp.arange(MAXP, dtype=jnp.int32)[None, :] < pages_used[:, None]
    matches = (
        (page_table[:, :, None] == jnp.arange(pool_size, dtype=jnp.int32)[None, None, :])
        & live_page[:, :, None]
    ).astype(jnp.int32)
    owner_table = jnp.sum(matches, axis=1)
    slot_ids = jnp.arange(slot_count, dtype=jnp.int32)
    page_owner = jnp.sum(owner_table * slot_ids[:, None], axis=0)
    page_rank = jnp.sum(matches * jnp.arange(MAXP, dtype=jnp.int32)[None, :, None], axis=(0, 1))
    page_limit = jnp.sum(owner_table * lengths[:, None], axis=0)
    offsets = page_rank[:, None] * PAGE + jnp.arange(PAGE, dtype=jnp.int32)[None, :]
    token_live = offsets < page_limit[:, None]
    page_queries = jnp.take(queries, page_owner, axis=0)
    scores = (
        jnp.einsum(
            "pgjd,pgdt->pgjt", page_queries, cache_pages[:, 0], preferred_element_type=jnp.float32
        )
        * score_scale
    )
    scores = jnp.where(token_live[:, None, None, :], scores, -jnp.inf)
    page_max = jnp.max(scores, axis=-1)
    own_score = (
        jnp.sum(queries.astype(jnp.float32) * own_key.astype(jnp.float32)[:, :, None, :], axis=-1)
        * score_scale
    )
    owner_mask = owner_table > 0
    slot_max = jnp.max(jnp.where(owner_mask[:, :, None, None], page_max[None], -jnp.inf), axis=1)
    slot_max = jnp.maximum(slot_max, own_score)
    weights = jnp.exp(scores - jnp.take(slot_max, page_owner, axis=0)[..., None])
    rounded = weights.astype(jnp.bfloat16)
    page_total = jnp.sum(weights, axis=-1)
    page_numerator = jnp.einsum(
        "pgjt,pgdt->pgjd", rounded, cache_pages[:, 1], preferred_element_type=jnp.float32
    )
    own_weight = jnp.exp(own_score - slot_max)
    own_rounded = lax.optimization_barrier(own_weight.astype(jnp.bfloat16)).astype(jnp.float32)
    owner_float = owner_table.astype(jnp.float32)
    denominator = (
        jnp.einsum("sp,pgj->sgj", owner_float, page_total, precision=lax.Precision.HIGHEST)
        + own_weight
    )
    numerator = jnp.einsum(
        "sp,pgjd->sgjd", owner_float, page_numerator, precision=lax.Precision.HIGHEST
    )
    numerator = numerator + own_rounded[..., None] * own_value.astype(jnp.float32)[:, :, None, :]
    context = (numerator / denominator[..., None]).astype(jnp.bfloat16).reshape(slot_count, -1)
    gathered = exchange(context, "req")
    wanted = first_slot + slot_ids
    selector = (occupant[None, :] == wanted[:, None]).astype(jnp.bfloat16)
    attended = jnp.dot(selector, gathered, preferred_element_type=jnp.float32).astype(jnp.bfloat16)
    partial_value = lax.dot_general(
        attended, w_out, (((1,), (1,)), ((), ())), preferred_element_type=jnp.float32
    )
    kv_count = lax.axis_size("kv")
    col_share = partial_value.shape[1] // kv_count
    blocks = partial_value.reshape(slot_count, kv_count, col_share).transpose(1, 0, 2)
    summed = jnp.sum(lax.all_to_all(blocks, "kv", 0, 0), axis=0)
    residual = lax.dynamic_slice_in_dim(hidden_wide, lax.axis_index("kv") * col_share, col_share, 1)
    return (residual + summed).astype(jnp.bfloat16)


def solution(mesh):
    return jax.shard_map(
        per_device,
        mesh=mesh,
        in_specs=(
            P("req", None),
            P(),
            P(None, "kv"),
            P(None, "kv"),
            P("req", None, "kv", None, None),
            P("req"),
            P("req", None),
            P(),
        ),
        out_specs=P("req", "kv"),
        check_vma=False,
    )
```

```python
import math

import jax
import jax.numpy as jnp
from jax import lax
from jax.sharding import PartitionSpec as P

HD = 96
PAGE = 128
MAXP = 128
GROUP = 2


def exchange(rows, axis):
    count = lax.axis_size(axis)
    sent = jnp.broadcast_to(rows[None], (count,) + rows.shape)
    return lax.all_to_all(sent, axis, 0, 0).reshape(count * rows.shape[0], rows.shape[1])


def per_device(hidden, norm_gain, w_qkv, w_out, cache_pages, lengths, page_table, occupant):
    slot_count = hidden.shape[0]
    pool_size = cache_pages.shape[0]
    kv_local = cache_pages.shape[2]
    first_slot = lax.axis_index("req") * slot_count
    slot_ids = jnp.arange(slot_count, dtype=jnp.int32)
    hidden_wide = hidden.astype(jnp.float32)
    normed = (
        hidden_wide
        * lax.rsqrt(jnp.mean(hidden_wide * hidden_wide, axis=1, keepdims=True) + 1e-05)
        * norm_gain
    ).astype(jnp.bfloat16)
    served = lax.dynamic_slice_in_dim(occupant, first_slot, slot_count)
    own_rows = jnp.dot(normed, w_qkv, preferred_element_type=jnp.float32).astype(jnp.bfloat16)
    every_row = exchange(own_rows, "req")
    slot_rows = jnp.take(every_row, served, axis=0)
    slot_rows = slot_rows.reshape(slot_count, kv_local, GROUP + 2, HD)
    queries = slot_rows[:, :, :GROUP]
    own_key = slot_rows[:, :, GROUP]
    own_value = slot_rows[:, :, GROUP + 1]
    score_scale = 1.0 / math.sqrt(HD)
    pages_used = (lengths + PAGE - 1) // PAGE
    live_page = jnp.arange(MAXP, dtype=jnp.int32)[None, :] < pages_used[:, None]
    matches = (
        (page_table[:, :, None] == jnp.arange(pool_size, dtype=jnp.int32)[None, None, :])
        & live_page[:, :, None]
    ).astype(jnp.int32)
    owner_table = jnp.sum(matches, axis=1)
    page_owner = jnp.sum(owner_table * slot_ids[:, None], axis=0)
    page_rank = jnp.sum(matches * jnp.arange(MAXP, dtype=jnp.int32)[None, :, None], axis=(0, 1))
    page_limit = jnp.sum(owner_table * lengths[:, None], axis=0)
    offsets = page_rank[:, None] * PAGE + jnp.arange(PAGE, dtype=jnp.int32)[None, :]
    token_live = offsets < page_limit[:, None]
    slot_live = (page_owner[None, :, None] == slot_ids[:, None, None]) & token_live[None]
    scores = (
        jnp.einsum(
            "sgjd,pgdt->sgjpt", queries, cache_pages[:, 0], preferred_element_type=jnp.float32
        )
        * score_scale
    )
    scores = jnp.where(slot_live[:, None, None], scores, -jnp.inf)
    own_score = (
        jnp.sum(queries.astype(jnp.float32) * own_key.astype(jnp.float32)[:, :, None, :], axis=-1)
        * score_scale
    )
    slot_max = jnp.maximum(jnp.max(scores, axis=(-2, -1)), own_score)
    weights = jnp.exp(scores - slot_max[..., None, None])
    rounded = weights.astype(jnp.bfloat16)
    own_weight = jnp.exp(own_score - slot_max)
    own_rounded = lax.optimization_barrier(own_weight.astype(jnp.bfloat16)).astype(jnp.float32)
    denominator = jnp.sum(weights, axis=(-2, -1)) + own_weight
    numerator = jnp.einsum(
        "sgjpt,pgdt->sgjd", rounded, cache_pages[:, 1], preferred_element_type=jnp.float32
    )
    numerator = numerator + own_rounded[..., None] * own_value.astype(jnp.float32)[:, :, None, :]
    context = (numerator / denominator[..., None]).astype(jnp.bfloat16).reshape(slot_count, -1)
    gathered = exchange(context, "req")
    wanted = first_slot + slot_ids
    selector = (occupant[None, :] == wanted[:, None]).astype(jnp.bfloat16)
    attended = jnp.dot(selector, gathered, preferred_element_type=jnp.float32).astype(jnp.bfloat16)
    partial_value = lax.dot_general(
        attended, w_out, (((1,), (1,)), ((), ())), preferred_element_type=jnp.float32
    )
    kv_count = lax.axis_size("kv")
    col_share = partial_value.shape[1] // kv_count
    blocks = partial_value.reshape(slot_count, kv_count, col_share).transpose(1, 0, 2)
    summed = jnp.sum(lax.all_to_all(blocks, "kv", 0, 0), axis=0)
    residual = lax.dynamic_slice_in_dim(hidden_wide, lax.axis_index("kv") * col_share, col_share, 1)
    return (residual + summed).astype(jnp.bfloat16)


def solution(mesh):
    return jax.shard_map(
        per_device,
        mesh=mesh,
        in_specs=(
            P("req", None),
            P(),
            P(None, "kv"),
            P(None, "kv"),
            P("req", None, "kv", None, None),
            P("req"),
            P("req", None),
            P(),
        ),
        out_specs=P("req", "kv"),
        check_vma=False,
    )
```

```python
import math

import jax
import jax.numpy as jnp
from jax import lax
from jax.sharding import PartitionSpec as P

HD = 96
PAGE = 128
MAXP = 128
GROUP = 2


def exchange(rows, axis):
    count = lax.axis_size(axis)
    sent = jnp.broadcast_to(rows[None], (count,) + rows.shape)
    return lax.all_to_all(sent, axis, 0, 0).reshape(count * rows.shape[0], rows.shape[1])


def per_device(hidden, norm_gain, w_qkv, w_out, cache_pages, lengths, page_table, occupant):
    slot_count = hidden.shape[0]
    pool_size = cache_pages.shape[0]
    kv_local = cache_pages.shape[2]
    first_slot = lax.axis_index("req") * slot_count
    slot_ids = jnp.arange(slot_count, dtype=jnp.int32)
    hidden_wide = hidden.astype(jnp.float32)
    normed = (
        hidden_wide
        * lax.rsqrt(jnp.mean(hidden_wide * hidden_wide, axis=1, keepdims=True) + 1e-05)
        * norm_gain
    ).astype(jnp.bfloat16)
    served = lax.dynamic_slice_in_dim(occupant, first_slot, slot_count)
    own_rows = jnp.dot(normed, w_qkv, preferred_element_type=jnp.float32).astype(jnp.bfloat16)
    every_row = exchange(own_rows, "req")
    slot_rows = jnp.take(every_row, served, axis=0)
    slot_rows = slot_rows.reshape(slot_count, kv_local, GROUP + 2, HD)
    queries = slot_rows[:, :, :GROUP]
    own_key = slot_rows[:, :, GROUP]
    own_value = slot_rows[:, :, GROUP + 1]
    score_scale = 1.0 / math.sqrt(HD)
    pages_used = (lengths + PAGE - 1) // PAGE
    live_page = jnp.arange(MAXP, dtype=jnp.int32)[None, :] < pages_used[:, None]
    matches = (
        (page_table[:, :, None] == jnp.arange(pool_size, dtype=jnp.int32)[None, None, :])
        & live_page[:, :, None]
    ).astype(jnp.int32)
    owner_table = jnp.sum(matches, axis=1)
    page_owner = jnp.sum(owner_table * slot_ids[:, None], axis=0)
    page_rank = jnp.sum(matches * jnp.arange(MAXP, dtype=jnp.int32)[None, :, None], axis=(0, 1))
    page_limit = jnp.sum(owner_table * lengths[:, None], axis=0)
    offsets = page_rank[:, None] * PAGE + jnp.arange(PAGE, dtype=jnp.int32)[None, :]
    token_live = offsets < page_limit[:, None]
    slot_live = (page_owner[None, :, None] == slot_ids[:, None, None]) & token_live[None]
    scores = (
        jnp.einsum(
            "sgjd,pgdt->sgjpt", queries, cache_pages[:, 0], preferred_element_type=jnp.float32
        )
        * score_scale
    )
    scores = jnp.where(slot_live[:, None, None], scores, -jnp.inf)
    own_score = (
        jnp.sum(queries.astype(jnp.float32) * own_key.astype(jnp.float32)[:, :, None, :], axis=-1)
        * score_scale
    )
    slot_max = jnp.maximum(jnp.max(scores, axis=(-2, -1)), own_score)
    weights = jnp.exp(scores - slot_max[..., None, None])
    rounded = lax.optimization_barrier(weights.astype(jnp.bfloat16))
    own_weight = jnp.exp(own_score - slot_max)
    own_rounded = lax.optimization_barrier(own_weight.astype(jnp.bfloat16)).astype(jnp.float32)
    denominator = jnp.sum(weights, axis=(-2, -1)) + own_weight
    numerator = jnp.einsum(
        "sgjpt,pgdt->sgjd", rounded, cache_pages[:, 1], preferred_element_type=jnp.float32
    )
    numerator = numerator + own_rounded[..., None] * own_value.astype(jnp.float32)[:, :, None, :]
    context = (numerator / denominator[..., None]).astype(jnp.bfloat16).reshape(slot_count, -1)
    gathered = exchange(context, "req")
    wanted = first_slot + slot_ids
    selector = (occupant[None, :] == wanted[:, None]).astype(jnp.bfloat16)
    attended = jnp.dot(selector, gathered, preferred_element_type=jnp.float32).astype(jnp.bfloat16)
    kv_count = lax.axis_size("kv")
    col_share = w_out.shape[0] // kv_count
    blocks = jnp.einsum(
        "sa,kca->ksc",
        attended,
        w_out.reshape(kv_count, col_share, w_out.shape[1]),
        preferred_element_type=jnp.float32,
    )
    summed = jnp.sum(lax.all_to_all(blocks, "kv", 0, 0), axis=0)
    residual = lax.dynamic_slice_in_dim(hidden_wide, lax.axis_index("kv") * col_share, col_share, 1)
    return (residual + summed).astype(jnp.bfloat16)


def solution(mesh):
    return jax.shard_map(
        per_device,
        mesh=mesh,
        in_specs=(
            P("req", None),
            P(),
            P(None, "kv"),
            P(None, "kv"),
            P("req", None, "kv", None, None),
            P("req"),
            P("req", None),
            P(),
        ),
        out_specs=P("req", "kv"),
        check_vma=False,
    )
```

```python
import math

import jax
import jax.numpy as jnp
from jax import lax
from jax.sharding import PartitionSpec as P

HD = 96
PAGE = 128
MAXP = 128
GROUP = 2


def exchange(rows, axis):
    count = lax.axis_size(axis)
    sent = jnp.broadcast_to(rows[None], (count,) + rows.shape)
    return lax.all_to_all(sent, axis, 0, 0).reshape(count * rows.shape[0], rows.shape[1])


def per_device(hidden, norm_gain, w_qkv, w_out, cache_pages, lengths, page_table, occupant):
    slot_count = hidden.shape[0]
    pool_size = cache_pages.shape[0]
    kv_local = cache_pages.shape[2]
    first_slot = lax.axis_index("req") * slot_count
    slot_ids = jnp.arange(slot_count, dtype=jnp.int32)
    hidden_wide = hidden.astype(jnp.float32)
    normed = (
        hidden_wide
        * lax.rsqrt(jnp.mean(hidden_wide * hidden_wide, axis=1, keepdims=True) + 1e-05)
        * norm_gain
    ).astype(jnp.bfloat16)
    served = lax.dynamic_slice_in_dim(occupant, first_slot, slot_count)
    own_rows = jnp.dot(normed, w_qkv, preferred_element_type=jnp.float32).astype(jnp.bfloat16)
    every_row = exchange(own_rows, "req")
    slot_rows = jnp.take(every_row, served, axis=0)
    slot_rows = slot_rows.reshape(slot_count, kv_local, GROUP + 2, HD)
    queries = slot_rows[:, :, :GROUP]
    own_key = slot_rows[:, :, GROUP]
    own_value = slot_rows[:, :, GROUP + 1]
    score_scale = 1.0 / math.sqrt(HD)
    pages_used = (lengths + PAGE - 1) // PAGE
    live_page = jnp.arange(MAXP, dtype=jnp.int32)[None, :] < pages_used[:, None]
    matches = (
        (page_table[:, :, None] == jnp.arange(pool_size, dtype=jnp.int32)[None, None, :])
        & live_page[:, :, None]
    ).astype(jnp.int32)
    owner_table = jnp.sum(matches, axis=1)
    page_owner = jnp.sum(owner_table * slot_ids[:, None], axis=0)
    page_rank = jnp.sum(matches * jnp.arange(MAXP, dtype=jnp.int32)[None, :, None], axis=(0, 1))
    page_limit = jnp.sum(owner_table * lengths[:, None], axis=0)
    offsets = page_rank[:, None] * PAGE + jnp.arange(PAGE, dtype=jnp.int32)[None, :]
    token_live = offsets < page_limit[:, None]
    slot_live = (page_owner[None, :, None] == slot_ids[:, None, None]) & token_live[None]
    scores = (
        jnp.einsum(
            "sgjd,pgdt->sgjpt", queries, cache_pages[:, 0], preferred_element_type=jnp.float32
        )
        * score_scale
    )
    scores = jnp.where(slot_live[:, None, None], scores, -jnp.inf)
    own_score = (
        jnp.sum(queries.astype(jnp.float32) * own_key.astype(jnp.float32)[:, :, None, :], axis=-1)
        * score_scale
    )
    slot_max = jnp.maximum(jnp.max(scores, axis=(-2, -1)), own_score)
    weights = jnp.exp(scores - slot_max[..., None, None])
    rounded = lax.optimization_barrier(weights.astype(jnp.bfloat16))
    own_weight = jnp.exp(own_score - slot_max)
    own_rounded = lax.optimization_barrier(own_weight.astype(jnp.bfloat16)).astype(jnp.float32)
    denominator = jnp.sum(weights, axis=(-2, -1)) + own_weight
    numerator = jnp.einsum(
        "sgjpt,pgdt->sgjd", rounded, cache_pages[:, 1], preferred_element_type=jnp.float32
    )
    numerator = numerator + own_rounded[..., None] * own_value.astype(jnp.float32)[:, :, None, :]
    context = (numerator / denominator[..., None]).astype(jnp.bfloat16).reshape(slot_count, -1)
    kv_count = lax.axis_size("kv")
    col_share = w_out.shape[0] // kv_count
    blocks = jnp.einsum(
        "sa,kca->ksc",
        context,
        w_out.reshape(kv_count, col_share, w_out.shape[1]),
        preferred_element_type=jnp.float32,
    )
    slot_sums = jnp.sum(lax.all_to_all(blocks, "kv", 0, 0), axis=0)
    every_sum = exchange(slot_sums, "req")
    inverse = jnp.zeros_like(occupant).at[occupant].set(jnp.arange(occupant.shape[0], dtype=jnp.int32))
    wanted = lax.dynamic_slice_in_dim(inverse, first_slot, slot_count)
    summed = jnp.take(every_sum, wanted, axis=0)
    residual = lax.dynamic_slice_in_dim(hidden_wide, lax.axis_index("kv") * col_share, col_share, 1)
    return (residual + summed).astype(jnp.bfloat16)


def solution(mesh):
    return jax.shard_map(
        per_device,
        mesh=mesh,
        in_specs=(
            P("req", None),
            P(),
            P(None, "kv"),
            P(None, "kv"),
            P("req", None, "kv", None, None),
            P("req"),
            P("req", None),
            P(),
        ),
        out_specs=P("req", "kv"),
        check_vma=False,
    )
```

```python
import math

import jax
import jax.numpy as jnp
from jax import lax
from jax.experimental import pallas as pl
from jax.sharding import PartitionSpec as P

HD = 96
PAGE = 128
MAXP = 128
GROUP = 2


def _project_kernel(x_ref, g_ref, w_ref, o_ref):
    wide = x_ref[...].astype(jnp.float32)
    scale = lax.rsqrt(jnp.mean(wide * wide, axis=1, keepdims=True) + 1e-05)
    normed = (wide * scale * g_ref[...]).astype(jnp.bfloat16)
    rows = jnp.dot(normed, w_ref[...], preferred_element_type=jnp.float32).astype(jnp.bfloat16)
    o_ref[...] = jnp.broadcast_to(rows[None], o_ref.shape)


def exchange(rows, axis):
    count = lax.axis_size(axis)
    sent = jnp.broadcast_to(rows[None], (count,) + rows.shape)
    return lax.all_to_all(sent, axis, 0, 0).reshape(count * rows.shape[0], rows.shape[1])


def per_device(hidden, norm_gain, w_qkv, w_out, cache_pages, lengths, page_table, occupant):
    slot_count = hidden.shape[0]
    pool_size = cache_pages.shape[0]
    kv_local = cache_pages.shape[2]
    first_slot = lax.axis_index("req") * slot_count
    slot_ids = jnp.arange(slot_count, dtype=jnp.int32)
    hidden_wide = hidden.astype(jnp.float32)
    served = lax.dynamic_slice_in_dim(occupant, first_slot, slot_count)
    req_count = lax.axis_size("req")
    sent_rows = pl.pallas_call(
        _project_kernel,
        out_shape=jax.ShapeDtypeStruct((req_count, slot_count, w_qkv.shape[1]), jnp.bfloat16),
    )(hidden, norm_gain.reshape(1, -1), w_qkv)
    every_row = lax.all_to_all(sent_rows, "req", 0, 0).reshape(-1, w_qkv.shape[1])
    slot_rows = jnp.take(every_row, served, axis=0)
    slot_rows = slot_rows.reshape(slot_count, kv_local, GROUP + 2, HD)
    queries = slot_rows[:, :, :GROUP]
    own_key = slot_rows[:, :, GROUP]
    own_value = slot_rows[:, :, GROUP + 1]
    score_scale = 1.0 / math.sqrt(HD)
    pages_used = (lengths + PAGE - 1) // PAGE
    live_page = jnp.arange(MAXP, dtype=jnp.int32)[None, :] < pages_used[:, None]
    matches = (
        (page_table[:, :, None] == jnp.arange(pool_size, dtype=jnp.int32)[None, None, :])
        & live_page[:, :, None]
    ).astype(jnp.int32)
    owner_table = jnp.sum(matches, axis=1)
    page_owner = jnp.sum(owner_table * slot_ids[:, None], axis=0)
    page_rank = jnp.sum(matches * jnp.arange(MAXP, dtype=jnp.int32)[None, :, None], axis=(0, 1))
    page_limit = jnp.sum(owner_table * lengths[:, None], axis=0)
    offsets = page_rank[:, None] * PAGE + jnp.arange(PAGE, dtype=jnp.int32)[None, :]
    token_live = offsets < page_limit[:, None]
    slot_live = (page_owner[None, :, None] == slot_ids[:, None, None]) & token_live[None]
    scores = (
        jnp.einsum(
            "sgjd,pgdt->sgjpt", queries, cache_pages[:, 0], preferred_element_type=jnp.float32
        )
        * score_scale
    )
    scores = jnp.where(slot_live[:, None, None], scores, -jnp.inf)
    own_score = (
        jnp.sum(queries.astype(jnp.float32) * own_key.astype(jnp.float32)[:, :, None, :], axis=-1)
        * score_scale
    )
    slot_max = jnp.maximum(jnp.max(scores, axis=(-2, -1)), own_score)
    weights = jnp.exp(scores - slot_max[..., None, None])
    rounded = lax.optimization_barrier(weights.astype(jnp.bfloat16))
    own_weight = jnp.exp(own_score - slot_max)
    own_rounded = lax.optimization_barrier(own_weight.astype(jnp.bfloat16)).astype(jnp.float32)
    denominator = jnp.sum(weights, axis=(-2, -1)) + own_weight
    numerator = jnp.einsum(
        "sgjpt,pgdt->sgjd", rounded, cache_pages[:, 1], preferred_element_type=jnp.float32
    )
    numerator = numerator + own_rounded[..., None] * own_value.astype(jnp.float32)[:, :, None, :]
    context = (numerator / denominator[..., None]).astype(jnp.bfloat16).reshape(slot_count, -1)
    gathered = exchange(context, "req")
    wanted = first_slot + slot_ids
    selector = (occupant[None, :] == wanted[:, None]).astype(jnp.bfloat16)
    attended = jnp.dot(selector, gathered, preferred_element_type=jnp.float32).astype(jnp.bfloat16)
    kv_count = lax.axis_size("kv")
    col_share = w_out.shape[0] // kv_count
    blocks = jnp.einsum(
        "sa,kca->ksc",
        attended,
        w_out.reshape(kv_count, col_share, w_out.shape[1]),
        preferred_element_type=jnp.float32,
    )
    summed = jnp.sum(lax.all_to_all(blocks, "kv", 0, 0), axis=0)
    residual = lax.dynamic_slice_in_dim(hidden_wide, lax.axis_index("kv") * col_share, col_share, 1)
    return (residual + summed).astype(jnp.bfloat16)


def solution(mesh):
    return jax.shard_map(
        per_device,
        mesh=mesh,
        in_specs=(
            P("req", None),
            P(),
            P(None, "kv"),
            P(None, "kv"),
            P("req", None, "kv", None, None),
            P("req"),
            P("req", None),
            P(),
        ),
        out_specs=P("req", "kv"),
        check_vma=False,
    )
```

```python
import math

import jax
import jax.numpy as jnp
from jax import lax
from jax.experimental import pallas as pl
from jax.sharding import PartitionSpec as P

HD = 96
PAGE = 128
MAXP = 128
GROUP = 2


def _project_kernel(x_ref, g_ref, w_ref, o_ref):
    wide = x_ref[...].astype(jnp.float32)
    scale = lax.rsqrt(jnp.mean(wide * wide, axis=1, keepdims=True) + 1e-05)
    normed = (wide * scale * g_ref[...]).astype(jnp.bfloat16)
    rows = jnp.dot(normed, w_ref[...], preferred_element_type=jnp.float32).astype(jnp.bfloat16)
    o_ref[...] = jnp.broadcast_to(rows[None], o_ref.shape)


def exchange(rows, axis):
    count = lax.axis_size(axis)
    sent = jnp.broadcast_to(rows[None], (count,) + rows.shape)
    return lax.all_to_all(sent, axis, 0, 0).reshape(count * rows.shape[0], rows.shape[1])


def per_device(hidden, norm_gain, w_qkv, w_out, cache_pages, lengths, page_table, occupant):
    slot_count = hidden.shape[0]
    pool_size = cache_pages.shape[0]
    kv_local = cache_pages.shape[2]
    first_slot = lax.axis_index("req") * slot_count
    slot_ids = jnp.arange(slot_count, dtype=jnp.int32)
    hidden_wide = hidden.astype(jnp.float32)
    served = lax.dynamic_slice_in_dim(occupant, first_slot, slot_count)
    req_count = lax.axis_size("req")
    sent_rows = pl.pallas_call(
        _project_kernel,
        out_shape=jax.ShapeDtypeStruct((req_count, slot_count, w_qkv.shape[1]), jnp.bfloat16),
    )(hidden, norm_gain, w_qkv)
    every_row = lax.all_to_all(sent_rows, "req", 0, 0).reshape(-1, w_qkv.shape[1])
    slot_rows = jnp.take(every_row, served, axis=0)
    slot_rows = slot_rows.reshape(slot_count, kv_local, GROUP + 2, HD)
    queries = slot_rows[:, :, :GROUP]
    own_key = slot_rows[:, :, GROUP]
    own_value = slot_rows[:, :, GROUP + 1]
    score_scale = 1.0 / math.sqrt(HD)
    pages_used = (lengths + PAGE - 1) // PAGE
    live_page = jnp.arange(MAXP, dtype=jnp.int32)[None, :] < pages_used[:, None]
    matches = (
        (page_table[:, :, None] == jnp.arange(pool_size, dtype=jnp.int32)[None, None, :])
        & live_page[:, :, None]
    ).astype(jnp.int32)
    owner_table = jnp.sum(matches, axis=1)
    page_owner = jnp.sum(owner_table * slot_ids[:, None], axis=0)
    page_rank = jnp.sum(matches * jnp.arange(MAXP, dtype=jnp.int32)[None, :, None], axis=(0, 1))
    page_limit = jnp.sum(owner_table * lengths[:, None], axis=0)
    offsets = page_rank[:, None] * PAGE + jnp.arange(PAGE, dtype=jnp.int32)[None, :]
    token_live = offsets < page_limit[:, None]
    slot_live = (page_owner[None, :, None] == slot_ids[:, None, None]) & token_live[None]
    scores = (
        jnp.einsum(
            "sgjd,pgdt->sgjpt", queries, cache_pages[:, 0], preferred_element_type=jnp.float32
        )
        * score_scale
    )
    scores = jnp.where(slot_live[:, None, None], scores, -jnp.inf)
    own_score = (
        jnp.sum(queries.astype(jnp.float32) * own_key.astype(jnp.float32)[:, :, None, :], axis=-1)
        * score_scale
    )
    slot_max = jnp.maximum(jnp.max(scores, axis=(-2, -1)), own_score)
    weights = jnp.exp(scores - slot_max[..., None, None])
    rounded = lax.optimization_barrier(weights.astype(jnp.bfloat16))
    own_weight = jnp.exp(own_score - slot_max)
    own_rounded = lax.optimization_barrier(own_weight.astype(jnp.bfloat16)).astype(jnp.float32)
    denominator = jnp.sum(weights, axis=(-2, -1)) + own_weight
    numerator = jnp.einsum(
        "sgjpt,pgdt->sgjd", rounded, cache_pages[:, 1], preferred_element_type=jnp.float32
    )
    numerator = numerator + own_rounded[..., None] * own_value.astype(jnp.float32)[:, :, None, :]
    context = (numerator / denominator[..., None]).astype(jnp.bfloat16).reshape(slot_count, -1)
    gathered = exchange(context, "req")
    wanted = first_slot + slot_ids
    selector = (occupant[None, :] == wanted[:, None]).astype(jnp.bfloat16)
    attended = jnp.dot(selector, gathered, preferred_element_type=jnp.float32).astype(jnp.bfloat16)
    kv_count = lax.axis_size("kv")
    col_share = w_out.shape[0] // kv_count
    blocks = jnp.einsum(
        "sa,kca->ksc",
        attended,
        w_out.reshape(kv_count, col_share, w_out.shape[1]),
        preferred_element_type=jnp.float32,
    )
    summed = jnp.sum(lax.all_to_all(blocks, "kv", 0, 0), axis=0)
    residual = lax.dynamic_slice_in_dim(hidden_wide, lax.axis_index("kv") * col_share, col_share, 1)
    return (residual + summed).astype(jnp.bfloat16)


def solution(mesh):
    return jax.shard_map(
        per_device,
        mesh=mesh,
        in_specs=(
            P("req", None),
            P(),
            P(None, "kv"),
            P(None, "kv"),
            P("req", None, "kv", None, None),
            P("req"),
            P("req", None),
            P(),
        ),
        out_specs=P("req", "kv"),
        check_vma=False,
    )
```

```python
import math

import jax
import jax.numpy as jnp
from jax import lax
from jax.experimental import pallas as pl
from jax.sharding import PartitionSpec as P

HD = 96
PAGE = 128
MAXP = 128
GROUP = 2


def _project_kernel(x_ref, g_ref, w_ref, o_ref):
    wide = x_ref[...].astype(jnp.float32)
    scale = lax.rsqrt(jnp.mean(wide * wide, axis=1, keepdims=True) + 1e-05)
    normed = (wide * scale * g_ref[...]).astype(jnp.bfloat16)
    rows = jnp.dot(normed, w_ref[...], preferred_element_type=jnp.float32).astype(jnp.bfloat16)
    o_ref[...] = jnp.broadcast_to(rows[None], o_ref.shape)


def exchange(rows, axis):
    count = lax.axis_size(axis)
    sent = jnp.broadcast_to(rows[None], (count,) + rows.shape)
    return lax.all_to_all(sent, axis, 0, 0).reshape(count * rows.shape[0], rows.shape[1])


def per_device(hidden, norm_gain, w_qkv, w_out, cache_pages, lengths, page_table, occupant):
    slot_count = hidden.shape[0]
    pool_size = cache_pages.shape[0]
    kv_local = cache_pages.shape[2]
    first_slot = lax.axis_index("req") * slot_count
    slot_ids = jnp.arange(slot_count, dtype=jnp.int32)
    hidden_wide = hidden.astype(jnp.float32)
    served = lax.dynamic_slice_in_dim(occupant, first_slot, slot_count)
    req_count = lax.axis_size("req")
    sent_rows = pl.pallas_call(
        _project_kernel,
        out_shape=jax.ShapeDtypeStruct((req_count, slot_count, w_qkv.shape[1]), jnp.bfloat16),
    )(hidden, norm_gain, w_qkv)
    every_row = lax.all_to_all(sent_rows, "req", 0, 0).reshape(-1, w_qkv.shape[1])
    slot_rows = jnp.take(every_row, served, axis=0)
    slot_rows = slot_rows.reshape(slot_count, kv_local, GROUP + 2, HD)
    queries = slot_rows[:, :, :GROUP]
    own_key = slot_rows[:, :, GROUP]
    own_value = slot_rows[:, :, GROUP + 1]
    score_scale = 1.0 / math.sqrt(HD)
    pages_used = (lengths + PAGE - 1) // PAGE
    live_page = jnp.arange(MAXP, dtype=jnp.int32)[None, :] < pages_used[:, None]
    matches = (
        (page_table[:, :, None] == jnp.arange(pool_size, dtype=jnp.int32)[None, None, :])
        & live_page[:, :, None]
    ).astype(jnp.int32)
    owner_table = jnp.sum(matches, axis=1)
    page_owner = jnp.sum(owner_table * slot_ids[:, None], axis=0)
    page_rank = jnp.sum(matches * jnp.arange(MAXP, dtype=jnp.int32)[None, :, None], axis=(0, 1))
    page_limit = jnp.sum(owner_table * lengths[:, None], axis=0)
    offsets = page_rank[:, None] * PAGE + jnp.arange(PAGE, dtype=jnp.int32)[None, :]
    token_live = offsets < page_limit[:, None]
    slot_live = (page_owner[None, :, None] == slot_ids[:, None, None]) & token_live[None]
    scores = (
        jnp.einsum(
            "sgjd,pgdt->sgjpt", queries, cache_pages[:, 0], preferred_element_type=jnp.float32
        )
        * score_scale
    )
    scores = jnp.where(slot_live[:, None, None], scores, -jnp.inf)
    own_score = (
        jnp.sum(queries.astype(jnp.float32) * own_key.astype(jnp.float32)[:, :, None, :], axis=-1)
        * score_scale
    )
    slot_max = jnp.maximum(jnp.max(scores, axis=(-2, -1)), own_score)
    weights = jnp.exp(scores - slot_max[..., None, None])
    rounded = lax.optimization_barrier(weights.astype(jnp.bfloat16))
    own_weight = jnp.exp(own_score - slot_max)
    own_rounded = lax.optimization_barrier(own_weight.astype(jnp.bfloat16)).astype(jnp.float32)
    denominator = jnp.sum(weights, axis=(-2, -1)) + own_weight
    numerator = jnp.einsum(
        "sgjpt,pgdt->sgjd", rounded, cache_pages[:, 1], preferred_element_type=jnp.float32
    )
    numerator = numerator + own_rounded[..., None] * own_value.astype(jnp.float32)[:, :, None, :]
    context = (numerator / denominator[..., None]).astype(jnp.bfloat16).reshape(slot_count, -1)
    gathered = exchange(context, "req")
    wanted = first_slot + slot_ids
    selector = (occupant[None, :] == wanted[:, None]).astype(jnp.bfloat16)
    attended = jnp.dot(selector, gathered, preferred_element_type=jnp.float32).astype(jnp.bfloat16)
    kv_count = lax.axis_size("kv")
    col_share = w_out.shape[0] // kv_count
    blocks = jnp.einsum(
        "sa,kca->ksc",
        attended,
        w_out.reshape(kv_count, col_share, w_out.shape[1]),
        preferred_element_type=jnp.float32,
    )
    summed = jnp.sum(lax.all_to_all(blocks, "kv", 0, 0), axis=0)
    residual = lax.dynamic_slice_in_dim(hidden_wide, lax.axis_index("kv") * col_share, col_share, 1)
    residual = lax.optimization_barrier(residual)
    return (residual + summed).astype(jnp.bfloat16)


def solution(mesh):
    return jax.shard_map(
        per_device,
        mesh=mesh,
        in_specs=(
            P("req", None),
            P(),
            P(None, "kv"),
            P(None, "kv"),
            P("req", None, "kv", None, None),
            P("req"),
            P("req", None),
            P(),
        ),
        out_specs=P("req", "kv"),
        check_vma=False,
    )
```

```python
import math

import jax
import jax.numpy as jnp
from jax import lax
from jax.experimental import pallas as pl
from jax.sharding import PartitionSpec as P

HD = 96
PAGE = 128
MAXP = 128
GROUP = 2


def _project_kernel(x_ref, g_ref, w_ref, o_ref):
    wide = x_ref[...].astype(jnp.float32)
    scale = lax.rsqrt(jnp.mean(wide * wide, axis=1, keepdims=True) + 1e-05)
    normed = (wide * scale * g_ref[...]).astype(jnp.bfloat16)
    rows = jnp.dot(normed, w_ref[...], preferred_element_type=jnp.float32).astype(jnp.bfloat16)
    o_ref[...] = jnp.broadcast_to(rows[None], o_ref.shape)


def exchange(rows, axis):
    count = lax.axis_size(axis)
    sent = jnp.broadcast_to(rows[None], (count,) + rows.shape)
    return lax.all_to_all(sent, axis, 0, 0).reshape(count * rows.shape[0], rows.shape[1])


def per_device(hidden, norm_gain, w_qkv, w_out, cache_pages, lengths, page_table, occupant):
    slot_count = hidden.shape[0]
    pool_size = cache_pages.shape[0]
    kv_local = cache_pages.shape[2]
    first_slot = lax.axis_index("req") * slot_count
    slot_ids = jnp.arange(slot_count, dtype=jnp.int32)
    hidden_wide = hidden.astype(jnp.float32)
    served = lax.dynamic_slice_in_dim(occupant, first_slot, slot_count)
    req_count = lax.axis_size("req")
    sent_rows = pl.pallas_call(
        _project_kernel,
        out_shape=jax.ShapeDtypeStruct((req_count, slot_count, w_qkv.shape[1]), jnp.bfloat16),
    )(hidden, norm_gain, w_qkv)
    every_row = lax.all_to_all(sent_rows, "req", 0, 0).reshape(-1, w_qkv.shape[1])
    slot_rows = jnp.take(every_row, served, axis=0)
    slot_rows = slot_rows.reshape(slot_count, kv_local, GROUP + 2, HD)
    queries = slot_rows[:, :, :GROUP]
    own_key = slot_rows[:, :, GROUP]
    own_value = slot_rows[:, :, GROUP + 1]
    score_scale = 1.0 / math.sqrt(HD)
    pages_used = (lengths + PAGE - 1) // PAGE
    live_page = jnp.arange(MAXP, dtype=jnp.int32)[None, :] < pages_used[:, None]
    matches = (
        (page_table[:, :, None] == jnp.arange(pool_size, dtype=jnp.int32)[None, None, :])
        & live_page[:, :, None]
    ).astype(jnp.int32)
    owner_table = jnp.sum(matches, axis=1)
    page_owner = jnp.sum(owner_table * slot_ids[:, None], axis=0)
    page_rank = jnp.sum(matches * jnp.arange(MAXP, dtype=jnp.int32)[None, :, None], axis=(0, 1))
    page_limit = jnp.sum(owner_table * lengths[:, None], axis=0)
    offsets = page_rank[:, None] * PAGE + jnp.arange(PAGE, dtype=jnp.int32)[None, :]
    token_live = offsets < page_limit[:, None]
    slot_live = (page_owner[None, :, None] == slot_ids[:, None, None]) & token_live[None]
    scores = (
        jnp.einsum(
            "sgjd,pgdt->sgjpt", queries, cache_pages[:, 0], preferred_element_type=jnp.float32
        )
        * score_scale
    )
    scores = jnp.where(slot_live[:, None, None], scores, -jnp.inf)
    own_score = (
        jnp.sum(queries.astype(jnp.float32) * own_key.astype(jnp.float32)[:, :, None, :], axis=-1)
        * score_scale
    )
    slot_max = jnp.maximum(jnp.max(scores, axis=(-2, -1)), own_score)
    weights = jnp.exp(scores - slot_max[..., None, None])
    rounded = lax.optimization_barrier(weights.astype(jnp.bfloat16))
    own_weight = jnp.exp(own_score - slot_max)
    own_rounded = lax.optimization_barrier(own_weight.astype(jnp.bfloat16)).astype(jnp.float32)
    denominator = jnp.sum(weights, axis=(-2, -1)) + own_weight
    numerator = jnp.einsum(
        "sgjpt,pgdt->sgjd", rounded, cache_pages[:, 1], preferred_element_type=jnp.float32
    )
    numerator = numerator + own_rounded[..., None] * own_value.astype(jnp.float32)[:, :, None, :]
    context = (
        jnp.broadcast_to(numerator[None], (req_count,) + numerator.shape)
        / denominator[None, ..., None]
    ).astype(jnp.bfloat16)
    gathered = lax.all_to_all(context, "req", 0, 0).reshape((-1,) + numerator.shape[1:])
    wanted = first_slot + slot_ids
    selector = (occupant[None, :] == wanted[:, None]).astype(jnp.bfloat16)
    attended = jnp.einsum(
        "rn,ngjd->rgjd", selector, gathered, preferred_element_type=jnp.float32
    ).astype(jnp.bfloat16)
    kv_count = lax.axis_size("kv")
    col_share = w_out.shape[0] // kv_count
    blocks = jnp.einsum(
        "sgjd,kcgjd->ksc",
        attended,
        w_out.reshape((kv_count, col_share) + numerator.shape[1:]),
        preferred_element_type=jnp.float32,
    )
    summed = jnp.sum(lax.all_to_all(blocks, "kv", 0, 0), axis=0)
    residual = lax.dynamic_slice_in_dim(hidden_wide, lax.axis_index("kv") * col_share, col_share, 1)
    residual = lax.optimization_barrier(residual)
    return (residual + summed).astype(jnp.bfloat16)


def solution(mesh):
    return jax.shard_map(
        per_device,
        mesh=mesh,
        in_specs=(
            P("req", None),
            P(),
            P(None, "kv"),
            P(None, "kv"),
            P("req", None, "kv", None, None),
            P("req"),
            P("req", None),
            P(),
        ),
        out_specs=P("req", "kv"),
        check_vma=False,
    )
```

```python
import math

import jax
import jax.numpy as jnp
from jax import lax
from jax.experimental import pallas as pl
from jax.sharding import PartitionSpec as P

HD = 96
PAGE = 128
MAXP = 128
GROUP = 2


def _project_kernel(x_ref, g_ref, w_ref, occ_ref, own_ref, o_ref):
    wide = x_ref[...].astype(jnp.float32)
    scale = lax.rsqrt(jnp.mean(wide * wide, axis=1, keepdims=True) + 1e-05)
    normed = (wide * scale * g_ref[...]).astype(jnp.bfloat16)
    rows = jnp.dot(normed, w_ref[...], preferred_element_type=jnp.float32).astype(jnp.bfloat16)
    route = (occ_ref[...] == own_ref[...]).astype(jnp.bfloat16)
    placed = jnp.dot(route, rows, preferred_element_type=jnp.float32).astype(jnp.bfloat16)
    o_ref[...] = placed.reshape(o_ref.shape)


def exchange(rows, axis):
    count = lax.axis_size(axis)
    sent = jnp.broadcast_to(rows[None], (count,) + rows.shape)
    return lax.all_to_all(sent, axis, 0, 0).reshape(count * rows.shape[0], rows.shape[1])


def per_device(hidden, norm_gain, w_qkv, w_out, cache_pages, lengths, page_table, occupant):
    slot_count = hidden.shape[0]
    pool_size = cache_pages.shape[0]
    kv_local = cache_pages.shape[2]
    first_slot = lax.axis_index("req") * slot_count
    slot_ids = jnp.arange(slot_count, dtype=jnp.int32)
    hidden_wide = hidden.astype(jnp.float32)
    req_count = lax.axis_size("req")
    sent_rows = pl.pallas_call(
        _project_kernel,
        out_shape=jax.ShapeDtypeStruct((req_count, slot_count, w_qkv.shape[1]), jnp.bfloat16),
    )(
        hidden,
        norm_gain,
        w_qkv,
        occupant.reshape(-1, 1),
        (first_slot + slot_ids).reshape(1, -1),
    )
    arrived = lax.all_to_all(sent_rows, "req", 0, 0)
    slot_rows = jnp.sum(arrived.astype(jnp.float32), axis=0).astype(jnp.bfloat16)
    slot_rows = slot_rows.reshape(slot_count, kv_local, GROUP + 2, HD)
    queries = slot_rows[:, :, :GROUP]
    own_key = slot_rows[:, :, GROUP]
    own_value = slot_rows[:, :, GROUP + 1]
    score_scale = 1.0 / math.sqrt(HD)
    pages_used = (lengths + PAGE - 1) // PAGE
    live_page = jnp.arange(MAXP, dtype=jnp.int32)[None, :] < pages_used[:, None]
    matches = (
        (page_table[:, :, None] == jnp.arange(pool_size, dtype=jnp.int32)[None, None, :])
        & live_page[:, :, None]
    ).astype(jnp.int32)
    owner_table = jnp.sum(matches, axis=1)
    page_owner = jnp.sum(owner_table * slot_ids[:, None], axis=0)
    page_rank = jnp.sum(matches * jnp.arange(MAXP, dtype=jnp.int32)[None, :, None], axis=(0, 1))
    page_limit = jnp.sum(owner_table * lengths[:, None], axis=0)
    offsets = page_rank[:, None] * PAGE + jnp.arange(PAGE, dtype=jnp.int32)[None, :]
    token_live = offsets < page_limit[:, None]
    slot_live = (page_owner[None, :, None] == slot_ids[:, None, None]) & token_live[None]
    scores = (
        jnp.einsum(
            "sgjd,pgdt->sgjpt", queries, cache_pages[:, 0], preferred_element_type=jnp.float32
        )
        * score_scale
    )
    scores = jnp.where(slot_live[:, None, None], scores, -jnp.inf)
    own_score = (
        jnp.sum(queries.astype(jnp.float32) * own_key.astype(jnp.float32)[:, :, None, :], axis=-1)
        * score_scale
    )
    slot_max = jnp.maximum(jnp.max(scores, axis=(-2, -1)), own_score)
    weights = jnp.exp(scores - slot_max[..., None, None])
    rounded = lax.optimization_barrier(weights.astype(jnp.bfloat16))
    own_weight = jnp.exp(own_score - slot_max)
    own_rounded = lax.optimization_barrier(own_weight.astype(jnp.bfloat16)).astype(jnp.float32)
    denominator = jnp.sum(weights, axis=(-2, -1)) + own_weight
    numerator = jnp.einsum(
        "sgjpt,pgdt->sgjd", rounded, cache_pages[:, 1], preferred_element_type=jnp.float32
    )
    numerator = numerator + own_rounded[..., None] * own_value.astype(jnp.float32)[:, :, None, :]
    context = (
        jnp.broadcast_to(numerator[None], (req_count,) + numerator.shape)
        / denominator[None, ..., None]
    ).astype(jnp.bfloat16)
    gathered = lax.all_to_all(context, "req", 0, 0).reshape((-1,) + numerator.shape[1:])
    wanted = first_slot + slot_ids
    selector = (occupant[None, :] == wanted[:, None]).astype(jnp.bfloat16)
    attended = jnp.einsum(
        "rn,ngjd->rgjd", selector, gathered, preferred_element_type=jnp.float32
    ).astype(jnp.bfloat16)
    kv_count = lax.axis_size("kv")
    col_share = w_out.shape[0] // kv_count
    blocks = jnp.einsum(
        "sgjd,kcgjd->ksc",
        attended,
        w_out.reshape((kv_count, col_share) + numerator.shape[1:]),
        preferred_element_type=jnp.float32,
    )
    summed = jnp.sum(lax.all_to_all(blocks, "kv", 0, 0), axis=0)
    residual = lax.dynamic_slice_in_dim(hidden_wide, lax.axis_index("kv") * col_share, col_share, 1)
    residual = lax.optimization_barrier(residual)
    return (residual + summed).astype(jnp.bfloat16)


def solution(mesh):
    return jax.shard_map(
        per_device,
        mesh=mesh,
        in_specs=(
            P("req", None),
            P(),
            P(None, "kv"),
            P(None, "kv"),
            P("req", None, "kv", None, None),
            P("req"),
            P("req", None),
            P(),
        ),
        out_specs=P("req", "kv"),
        check_vma=False,
    )
```

```python
import math

import jax
import jax.numpy as jnp
from jax import lax
from jax.experimental import pallas as pl
from jax.sharding import PartitionSpec as P

HD = 96
PAGE = 128
MAXP = 128
GROUP = 2


def _project_kernel(x_ref, g_ref, w_ref, o_ref):
    wide = x_ref[...].astype(jnp.float32)
    scale = lax.rsqrt(jnp.mean(wide * wide, axis=1, keepdims=True) + 1e-05)
    normed = (wide * scale * g_ref[...]).astype(jnp.bfloat16)
    rows = jnp.dot(normed, w_ref[...], preferred_element_type=jnp.float32).astype(jnp.bfloat16)
    o_ref[...] = jnp.broadcast_to(rows[None], o_ref.shape)


def exchange(rows, axis):
    count = lax.axis_size(axis)
    sent = jnp.broadcast_to(rows[None], (count,) + rows.shape)
    return lax.all_to_all(sent, axis, 0, 0).reshape(count * rows.shape[0], rows.shape[1])


def per_device(hidden, norm_gain, w_qkv, w_out, cache_pages, lengths, page_table, occupant):
    slot_count = hidden.shape[0]
    pool_size = cache_pages.shape[0]
    kv_local = cache_pages.shape[2]
    first_slot = lax.axis_index("req") * slot_count
    slot_ids = jnp.arange(slot_count, dtype=jnp.int32)
    hidden_wide = hidden.astype(jnp.float32)
    served = lax.dynamic_slice_in_dim(occupant, first_slot, slot_count)
    req_count = lax.axis_size("req")
    sent_rows = pl.pallas_call(
        _project_kernel,
        out_shape=jax.ShapeDtypeStruct((req_count, slot_count, w_qkv.shape[1]), jnp.bfloat16),
    )(hidden, norm_gain, w_qkv)
    every_row = lax.all_to_all(sent_rows, "req", 0, 0).reshape(-1, w_qkv.shape[1])
    picker = (served[:, None] == jnp.arange(every_row.shape[0], dtype=jnp.int32)[None, :])
    slot_rows = jnp.dot(
        picker.astype(jnp.bfloat16), every_row, preferred_element_type=jnp.float32
    ).astype(jnp.bfloat16)
    slot_rows = slot_rows.reshape(slot_count, kv_local, GROUP + 2, HD)
    queries = slot_rows[:, :, :GROUP]
    own_key = slot_rows[:, :, GROUP]
    own_value = slot_rows[:, :, GROUP + 1]
    score_scale = 1.0 / math.sqrt(HD)
    pages_used = (lengths + PAGE - 1) // PAGE
    live_page = jnp.arange(MAXP, dtype=jnp.int32)[None, :] < pages_used[:, None]
    matches = (
        (page_table[:, :, None] == jnp.arange(pool_size, dtype=jnp.int32)[None, None, :])
        & live_page[:, :, None]
    ).astype(jnp.int32)
    owner_table = jnp.sum(matches, axis=1)
    page_owner = jnp.sum(owner_table * slot_ids[:, None], axis=0)
    page_rank = jnp.sum(matches * jnp.arange(MAXP, dtype=jnp.int32)[None, :, None], axis=(0, 1))
    page_limit = jnp.sum(owner_table * lengths[:, None], axis=0)
    offsets = page_rank[:, None] * PAGE + jnp.arange(PAGE, dtype=jnp.int32)[None, :]
    token_live = offsets < page_limit[:, None]
    slot_live = (page_owner[None, :, None] == slot_ids[:, None, None]) & token_live[None]
    scores = (
        jnp.einsum(
            "sgjd,pgdt->sgjpt", queries, cache_pages[:, 0], preferred_element_type=jnp.float32
        )
        * score_scale
    )
    scores = jnp.where(slot_live[:, None, None], scores, -jnp.inf)
    own_score = (
        jnp.sum(queries.astype(jnp.float32) * own_key.astype(jnp.float32)[:, :, None, :], axis=-1)
        * score_scale
    )
    slot_max = jnp.maximum(jnp.max(scores, axis=(-2, -1)), own_score)
    weights = jnp.exp(scores - slot_max[..., None, None])
    rounded = lax.optimization_barrier(weights.astype(jnp.bfloat16))
    own_weight = jnp.exp(own_score - slot_max)
    own_rounded = lax.optimization_barrier(own_weight.astype(jnp.bfloat16)).astype(jnp.float32)
    denominator = jnp.sum(weights, axis=(-2, -1)) + own_weight
    numerator = jnp.einsum(
        "sgjpt,pgdt->sgjd", rounded, cache_pages[:, 1], preferred_element_type=jnp.float32
    )
    numerator = numerator + own_rounded[..., None] * own_value.astype(jnp.float32)[:, :, None, :]
    context = (
        jnp.broadcast_to(numerator[None], (req_count,) + numerator.shape)
        / denominator[None, ..., None]
    ).astype(jnp.bfloat16)
    gathered = lax.all_to_all(context, "req", 0, 0).reshape((-1,) + numerator.shape[1:])
    wanted = first_slot + slot_ids
    selector = (occupant[None, :] == wanted[:, None]).astype(jnp.bfloat16)
    attended = jnp.einsum(
        "rn,ngjd->rgjd", selector, gathered, preferred_element_type=jnp.float32
    ).astype(jnp.bfloat16)
    kv_count = lax.axis_size("kv")
    col_share = w_out.shape[0] // kv_count
    blocks = jnp.einsum(
        "sgjd,kcgjd->ksc",
        attended,
        w_out.reshape((kv_count, col_share) + numerator.shape[1:]),
        preferred_element_type=jnp.float32,
    )
    summed = jnp.sum(lax.all_to_all(blocks, "kv", 0, 0), axis=0)
    residual = lax.dynamic_slice_in_dim(hidden_wide, lax.axis_index("kv") * col_share, col_share, 1)
    residual = lax.optimization_barrier(residual)
    return (residual + summed).astype(jnp.bfloat16)


def solution(mesh):
    return jax.shard_map(
        per_device,
        mesh=mesh,
        in_specs=(
            P("req", None),
            P(),
            P(None, "kv"),
            P(None, "kv"),
            P("req", None, "kv", None, None),
            P("req"),
            P("req", None),
            P(),
        ),
        out_specs=P("req", "kv"),
        check_vma=False,
    )
```
